32 devices in a mesh: snode: 16 (over z, y, x), row: 2 (over core).
Axes of the slice: x: 2, y: 2, z: 4, core: 2. Of those that a mesh axis runs over, the one named last changes fastest.
Arguments:
- ancestor_sigma: bfloat16 [8192, 8192], P('row', 'snode'), may hold values from -8 to 8, as said below
- child_panels: bfloat16 [96, 4096, 128], P('snode', 'row'), may hold values from -1 to 1
- diagonal_inverse_blocks: float32 [96, 128, 128], P('snode', 'row'), may hold values from -4 to 4, as said below
- block_list: int32 [96, 32], P('snode'), may hold values from 0 to 63, as said below
- block_count: int32 [96], P('snode'), may hold values from 8 to 32, as said below
- child_width: int32 [96], P('snode'), may hold values from 64 to 128, as said below
- owner_slot: int32 [64], replicated, may hold values from 0 to 63, each once
Outputs:
- selected_panel_inverse: float32 [8192, 96, 128], P('row', 'snode')
- selected_diagonal_inverse: float32 [96, 128, 128], P('snode', 'row')
The draws below stay inside these ranges and needn't reach their ends.
Inputs may be any that keep to these rules, and one draw needn't show every extreme that they name: `ancestor_sigma`: symmetric. `diagonal_inverse_blocks`: each child's block is symmetric. `block_list`: the 32 entries of a row are distinct and ascending. `block_count`: some child has exactly 32. `child_width`: some child has exactly 128.
All inputs are finite; a program needn't handle non-finite values.
Results may differ from the reference program's by a relative error of at most 0.0003.
Values may be sent and summed in bfloat16 or wider, within the bound.
No kernel may reach another device: no remote copies, remote signals or barrier semaphores. Data moves between devices by JAX's collectives and lax.ppermute only.
A program may use at most 192 MiB of HBM per device.

```python
import jax
import jax.numpy as jnp
from jax import lax

B = 128
ANC = 4096
KMAX = 32
WJ = 128
SEP = 8192
NB = 64
CHILDREN = 96


def draw_ancestor_sigma(key, part):
    full_size = 2 * ANC
    noise_key, diag_key = jax.random.split(key, 2)
    noise_draw = jnp.clip(jax.random.normal(noise_key, (full_size, full_size), jnp.float32), -6.0, 6.0)
    matrix = (noise_draw + noise_draw.T) * (1.4 / full_size ** 0.5)
    diagonal = jax.random.uniform(diag_key, (full_size,), jnp.float32, 0.5, 2.0)
    matrix = matrix + jnp.diag(diagonal)
    return matrix.astype(jnp.bfloat16)


def draw_diagonal_inverse_blocks(key, part):
    noise_draw = jnp.clip(jax.random.normal(key, (CHILDREN, WJ, WJ), jnp.float32), -6.0, 6.0)
    matrix = (noise_draw + jnp.swapaxes(noise_draw, 1, 2)) * 0.15
    return matrix + 2.0 * jnp.eye(WJ, dtype=jnp.float32)[None, :, :]


def draw_block_list(key, part):
    child_keys = jax.random.split(key, CHILDREN)

    def draw_row(row_key):
        ordering = jax.random.permutation(row_key, NB)[:KMAX]
        return jnp.sort(ordering)
    return jax.vmap(draw_row)(child_keys).astype(jnp.int32)


def draw_block_count(key, part):
    count_key, pick_key = jax.random.split(key)
    lowest = max(1, KMAX // 4)
    counts = jax.random.randint(count_key, (CHILDREN,), lowest, KMAX + 1)
    chosen = jax.random.randint(pick_key, (), 0, CHILDREN)
    return jnp.where(jnp.arange(CHILDREN) == chosen, KMAX, counts).astype(jnp.int32)


def draw_child_width(key, part):
    width_key, pick_key = jax.random.split(key)
    widths = jax.random.randint(width_key, (CHILDREN,), WJ // 2, WJ + 1)
    chosen = jax.random.randint(pick_key, (), 0, CHILDREN)
    return jnp.where(jnp.arange(CHILDREN) == chosen, WJ, widths).astype(jnp.int32)


def shard_levels(stream_key, extent, pieces, least, largest):
    def one(dim, shards_of):
        heights = jax.random.uniform(jax.random.fold_in(jax.random.fold_in(stream_key, 6), dim), (shards_of,), jnp.float32, least / len(pieces), largest / len(pieces))
        return jnp.repeat(jnp.exp(heights), extent[dim] // shards_of).reshape((-1,) + (1,) * (len(extent) - dim - 1))

    gain = one(*pieces[0])
    for cut in pieces[1:]:
        gain = gain * one(*cut)
    return gain


def normal_values(key, dims, width, reach, cuts=(), kind=jnp.bfloat16):
    array = jax.random.normal(key, dims, jnp.float32) * width
    if len(cuts) > 0:
        array = shard_levels(key, dims, cuts, -0.22, 0.18) * array
    return jnp.clip(array, min=-reach, max=reach).astype(kind)


def setup_inputs(seed: int = 0) -> dict:
    seeds = jax.random.split(jax.random.key(seed), 8)
    ancestor_sigma = draw_ancestor_sigma(jax.random.fold_in(seeds[7], 71), 0)
    child_panels = normal_values(seeds[1], (CHILDREN, KMAX * B, WJ), (4.0 / (KMAX * B) ** 0.5), 1.0, ((0, 16), (1, 2)))
    diagonal_inverse_blocks = draw_diagonal_inverse_blocks(jax.random.fold_in(seeds[7], 71), 0)
    block_list = draw_block_list(jax.random.fold_in(seeds[7], 71), 0)
    block_count = draw_block_count(jax.random.fold_in(seeds[7], 71), 0)
    child_width = draw_child_width(jax.random.fold_in(seeds[7], 71), 0)
    owner_slot = jax.random.permutation(seeds[6], NB).astype(jnp.int32)
    return dict(ancestor_sigma=ancestor_sigma, child_panels=child_panels, diagonal_inverse_blocks=diagonal_inverse_blocks, block_list=block_list, block_count=block_count, child_width=child_width, owner_slot=owner_slot)


def reference(ancestor_sigma, child_panels, diagonal_inverse_blocks, block_list, block_count, child_width, owner_slot):
    highest = lax.Precision.HIGHEST
    block_ids = jnp.arange(NB, dtype=jnp.int32)
    slot_ids = owner_slot[block_list].astype(jnp.int32)
    valid_blocks = jnp.arange(KMAX, dtype=jnp.int32)[None, :] < block_count[:, None]
    placed = ((slot_ids[:, :, None] == block_ids[None, None, :]) & valid_blocks[:, :, None]).astype(jnp.float32)
    active_columns = (jnp.arange(WJ, dtype=jnp.int32)[None, :] < child_width[:, None]).astype(jnp.float32)
    blocks = child_panels.astype(jnp.float32).reshape(CHILDREN, KMAX, B, WJ) * active_columns[:, None, None, :]
    full_panel = jnp.einsum("ckn,ckbj->nbcj", placed, blocks, precision=highest)
    full_panel = full_panel.astype(jnp.bfloat16).reshape(SEP, CHILDREN * WJ).astype(jnp.float32)
    product = jnp.dot(ancestor_sigma.astype(jnp.float32), full_panel, precision=highest)
    product_table = product.reshape(SEP, CHILDREN, WJ)
    diag_terms = jnp.einsum("nca,ncb->cab", full_panel.reshape(SEP, CHILDREN, WJ), product_table, precision=highest)
    slot_live = jnp.sum(placed, axis=1)
    active_rows = jnp.repeat(slot_live.T, B, axis=0)
    selected_panel_inverse = -product_table * active_rows[:, :, None] * active_columns[None, :, :]
    selected_diagonal_inverse = (diagonal_inverse_blocks + diag_terms) * active_columns[:, :, None] * active_columns[:, None, :]
    return selected_panel_inverse, selected_diagonal_inverse
```

```python
import numpy as np
import jax
import jax.numpy as jnp
from jax import lax
from jax.sharding import Mesh
from jax.sharding import PartitionSpec as P

B = 128
KMAX = 32
WJ = 128
NB = 64
GATHER_CHUNKS = 4


def slot_table(block_list, block_count, child_width, owner_slot):
    block_ids = jnp.arange(NB, dtype=jnp.int32)
    named = block_list[:, :, None] == block_ids[None, None, :]
    slot_ids = jnp.sum(jnp.where(named, owner_slot[None, None, :], 0), axis=2)
    valid_blocks = jnp.arange(KMAX, dtype=jnp.int32)[None, :] < block_count[:, None]
    placed = (slot_ids[:, :, None] == block_ids[None, None, :]) & valid_blocks[:, :, None]
    active_columns = jnp.arange(WJ, dtype=jnp.int32)[None, :] < child_width[:, None]
    return (placed, active_columns)


def expand_rows(place_table, blocks):
    children = blocks.shape[0]
    spread = jnp.einsum("ckn,ckbj->nbcj", place_table, blocks, preferred_element_type=jnp.float32)
    return spread.astype(jnp.bfloat16).reshape(place_table.shape[2] * B, children * WJ)


def masked_blocks(panels, active_columns):
    children = panels.shape[0]
    blocks = panels.reshape(children, KMAX, B, WJ)
    return jnp.where(active_columns[:, None, None, :], blocks, jnp.zeros_like(blocks))


def body(
    ancestor_sigma,
    child_panels,
    diagonal_inverse_blocks,
    block_list,
    block_count,
    child_width,
    owner_slot,
):
    row_devices = lax.axis_size("row")
    outer = lax.axis_size("so")
    row_positions = lax.axis_index("row")
    children = child_panels.shape[0]
    local_rows = ancestor_sigma.shape[0]
    swap = [(y * row_devices + x, x * row_devices + y) for x in range(row_devices) for y in range(outer)]

    own_panels = lax.all_gather(child_panels, "row", axis=1, tiled=True)
    far_panels = lax.ppermute(own_panels, ("so", "row"), swap)
    far_tables = lax.ppermute(
        jnp.concatenate([block_list, block_count[:, None], child_width[:, None]], axis=1),
        ("so", "row"),
        swap,
    )
    far_placed, far_active = slot_table(
        far_tables[:, :KMAX], far_tables[:, KMAX], far_tables[:, KMAX + 1], owner_slot
    )
    far_rows = expand_rows(far_placed.astype(jnp.bfloat16), masked_blocks(far_panels, far_active))

    chunk = local_rows // GATHER_CHUNKS
    far_rows = far_rows.reshape(row_devices, GATHER_CHUNKS, chunk, children * WJ)
    product = None
    for q in range(GATHER_CHUNKS):
        piece = lax.all_gather(ancestor_sigma[q * chunk : (q + 1) * chunk], "si", axis=1, tiled=True)
        piece = lax.all_gather(piece, "row", axis=0, tiled=True)
        rows_q = far_rows[:, q].reshape(row_devices * chunk, children * WJ)
        part = lax.dot_general(
            piece, rows_q, (((0,), (0,)), ((), ())), preferred_element_type=jnp.float32
        )
        product = part if product is None else product + part
    product = lax.ppermute(product, ("so", "row"), swap)
    product_table = product.reshape(local_rows, children, WJ)

    placed, active_columns = slot_table(block_list, block_count, child_width, owner_slot)
    place_bf = placed.astype(jnp.bfloat16)
    blocks = masked_blocks(own_panels, active_columns)
    own_blocks = local_rows // B
    own_table = lax.dynamic_slice_in_dim(place_bf, row_positions * own_blocks, own_blocks, 2)
    own_rows = expand_rows(own_table, blocks).reshape(local_rows, children, WJ).astype(jnp.float32)
    partial_value = jnp.einsum(
        "nca,ncb->cab", own_rows, product_table, precision=lax.Precision.HIGHEST
    )
    shared_rows = WJ // row_devices
    reduced_total = lax.psum(partial_value, "row")
    reduced_total = lax.dynamic_slice_in_dim(
        reduced_total, row_positions * shared_rows, shared_rows, 1
    )
    active_flags = active_columns.astype(jnp.float32)
    owned_active = lax.dynamic_slice_in_dim(
        active_flags, row_positions * shared_rows, shared_rows, 1
    )
    selected_diagonal_inverse = (
        (diagonal_inverse_blocks + reduced_total)
        * owned_active[:, :, None]
        * active_flags[:, None, :]
    )
    slot_live = jnp.sum(placed.astype(jnp.float32), axis=1)
    own_slots = lax.dynamic_slice_in_dim(slot_live, row_positions * own_blocks, own_blocks, 1)
    active_rows = jnp.repeat(own_slots.T, B, axis=0)
    selected_panel_inverse = -product_table * active_rows[:, :, None] * active_flags[None, :, :]
    return (selected_panel_inverse, selected_diagonal_inverse)


def solution(mesh):
    snodes = mesh.shape["snode"]
    rows = mesh.shape["row"]
    grid = Mesh(
        np.asarray(mesh.devices).reshape(rows, snodes // rows, rows), ("so", "si", "row")
    )
    sn = ("so", "si")
    placed = (
        P("row", sn),
        P(sn, "row", None),
        P(sn, "row", None),
        P(sn, None),
        P(sn),
        P(sn),
        P(),
    )
    return jax.shard_map(
        body,
        mesh=grid,
        in_specs=placed,
        out_specs=(P("row", sn, None), P(sn, "row", None)),
        check_vma=False,
    )
```

```python
import jax
import jax.numpy as jnp
from jax import lax
from jax.sharding import PartitionSpec as P

B = 128
KMAX = 32
WJ = 128
NB = 64
GATHER_CHUNKS = 4


def slot_table(block_list, block_count, child_width, owner_slot):
    block_ids = jnp.arange(NB, dtype=jnp.int32)
    named = block_list[:, :, None] == block_ids[None, None, :]
    slot_ids = jnp.sum(jnp.where(named, owner_slot[None, None, :], 0), axis=2)
    valid_blocks = jnp.arange(KMAX, dtype=jnp.int32)[None, :] < block_count[:, None]
    placed = (slot_ids[:, :, None] == block_ids[None, None, :]) & valid_blocks[:, :, None]
    active_columns = jnp.arange(WJ, dtype=jnp.int32)[None, :] < child_width[:, None]
    return (placed, active_columns)


def expand_rows(place_table, blocks):
    children = blocks.shape[0]
    spread = jnp.einsum("ckn,ckbj->nbcj", place_table, blocks, preferred_element_type=jnp.float32)
    return spread.astype(jnp.bfloat16).reshape(place_table.shape[2] * B, children * WJ)


def body(
    ancestor_sigma,
    child_panels,
    diagonal_inverse_blocks,
    block_list,
    block_count,
    child_width,
    owner_slot,
):
    row_devices = lax.axis_size("row")
    row_positions = lax.axis_index("row")
    children = child_panels.shape[0]
    local_rows = ancestor_sigma.shape[0]
    placed, active_columns = slot_table(block_list, block_count, child_width, owner_slot)
    place_bf = placed.astype(jnp.bfloat16)
    gathered = lax.all_gather(child_panels, "row", axis=1, tiled=True)
    blocks = gathered.reshape(children, KMAX, B, WJ)
    blocks = jnp.where(active_columns[:, None, None, :], blocks, jnp.zeros_like(blocks))
    panel_rows = expand_rows(place_bf, blocks)
    snode_devices = lax.axis_size("snode")
    own_cols = ancestor_sigma.shape[1]
    chunk = own_cols // GATHER_CHUNKS
    flipped = ancestor_sigma.T
    rows_by_chunk = panel_rows.reshape(snode_devices, GATHER_CHUNKS, chunk, children * WJ)
    product = None
    for q in range(GATHER_CHUNKS):
        piece = lax.all_gather(flipped[q * chunk : (q + 1) * chunk], "snode", axis=0, tiled=True)
        rows_q = rows_by_chunk[:, q].reshape(snode_devices * chunk, children * WJ)
        part = lax.dot_general(
            piece, rows_q, (((0,), (0,)), ((), ())), preferred_element_type=jnp.float32
        )
        product = part if product is None else product + part
    product_table = product.reshape(local_rows, children, WJ)
    own_blocks = local_rows // B
    own_table = lax.dynamic_slice_in_dim(place_bf, row_positions * own_blocks, own_blocks, 2)
    own_rows = expand_rows(own_table, blocks).reshape(local_rows, children, WJ).astype(jnp.float32)
    partial_value = jnp.einsum(
        "nca,ncb->cab", own_rows, product_table, precision=lax.Precision.HIGHEST
    )
    shared_rows = WJ // row_devices
    reduced_total = lax.psum(partial_value, "row")
    reduced_total = lax.dynamic_slice_in_dim(
        reduced_total, row_positions * shared_rows, shared_rows, 1
    )
    active_flags = active_columns.astype(jnp.float32)
    owned_active = lax.dynamic_slice_in_dim(
        active_flags, row_positions * shared_rows, shared_rows, 1
    )
    selected_diagonal_inverse = (
        (diagonal_inverse_blocks + reduced_total)
        * owned_active[:, :, None]
        * active_flags[:, None, :]
    )
    slot_live = jnp.sum(placed.astype(jnp.float32), axis=1)
    own_slots = lax.dynamic_slice_in_dim(slot_live, row_positions * own_blocks, own_blocks, 1)
    active_rows = jnp.repeat(own_slots.T, B, axis=0)
    selected_panel_inverse = -product_table * active_rows[:, :, None] * active_flags[None, :, :]
    return (selected_panel_inverse, selected_diagonal_inverse)


def solution(mesh):
    placed = (
        P("row", "snode"),
        P("snode", "row", None),
        P("snode", "row", None),
        P("snode", None),
        P("snode"),
        P("snode"),
        P(),
    )
    return jax.shard_map(
        body,
        mesh=mesh,
        in_specs=placed,
        out_specs=(P("row", "snode", None), P("snode", "row", None)),
        check_vma=False,
    )
```

```python
import jax
import jax.numpy as jnp
from jax import lax
from jax.sharding import PartitionSpec as P

B = 128
KMAX = 32
WJ = 128
NB = 64


def slot_table(block_list, block_count, child_width, owner_slot):
    block_ids = jnp.arange(NB, dtype=jnp.int32)
    named = block_list[:, :, None] == block_ids[None, None, :]
    slot_ids = jnp.sum(jnp.where(named, owner_slot[None, None, :], 0), axis=2)
    valid_blocks = jnp.arange(KMAX, dtype=jnp.int32)[None, :] < block_count[:, None]
    placed = (slot_ids[:, :, None] == block_ids[None, None, :]) & valid_blocks[:, :, None]
    active_columns = jnp.arange(WJ, dtype=jnp.int32)[None, :] < child_width[:, None]
    return (placed, active_columns)


def expand_rows(place_table, blocks):
    children = blocks.shape[0]
    spread = jnp.einsum("ckn,ckbj->nbcj", place_table, blocks, preferred_element_type=jnp.float32)
    return spread.astype(jnp.bfloat16).reshape(place_table.shape[2] * B, children * WJ)


def body(
    ancestor_sigma,
    child_panels,
    diagonal_inverse_blocks,
    block_list,
    block_count,
    child_width,
    owner_slot,
):
    row_devices = lax.axis_size("row")
    row_positions = lax.axis_index("row")
    children = child_panels.shape[0]
    local_rows = ancestor_sigma.shape[0]
    placed, active_columns = slot_table(block_list, block_count, child_width, owner_slot)
    place_bf = placed.astype(jnp.bfloat16)
    gathered = lax.all_gather(child_panels, "row", axis=1, tiled=True)
    blocks = gathered.reshape(children, KMAX, B, WJ)
    blocks = jnp.where(active_columns[:, None, None, :], blocks, jnp.zeros_like(blocks))
    panel_rows = expand_rows(place_bf, blocks)
    snode_devices = lax.axis_size("snode")
    snode_position = lax.axis_index("snode")
    own_cols = ancestor_sigma.shape[1]
    half = own_cols // 2
    by_block = panel_rows.reshape(snode_devices, own_cols, children * WJ)
    gathered_half = lax.all_gather(ancestor_sigma[:, :half], "snode", axis=1, tiled=True)
    product = jnp.dot(
        gathered_half,
        by_block[:, :half].reshape(snode_devices * half, children * WJ),
        preferred_element_type=jnp.float32,
    )
    rest = ancestor_sigma[:, half:]
    pieces = []
    rows = []
    for shift in range(snode_devices):
        if shift == 0:
            pieces.append(rest)
        else:
            pieces.append(
                lax.ppermute(
                    rest, "snode", [(i, (i + shift) % snode_devices) for i in range(snode_devices)]
                )
            )
        source = (snode_position - shift) % snode_devices
        rows.append(
            lax.dynamic_slice_in_dim(panel_rows, source * own_cols + half, own_cols - half, 0)
        )
    product = product + jnp.dot(
        jnp.concatenate(pieces, axis=1),
        jnp.concatenate(rows, axis=0),
        preferred_element_type=jnp.float32,
    )
    product_table = product.reshape(local_rows, children, WJ)
    own_blocks = local_rows // B
    own_table = lax.dynamic_slice_in_dim(place_bf, row_positions * own_blocks, own_blocks, 2)
    own_rows = expand_rows(own_table, blocks).reshape(local_rows, children, WJ).astype(jnp.float32)
    partial_value = jnp.einsum(
        "nca,ncb->cab", own_rows, product_table, precision=lax.Precision.HIGHEST
    )
    shared_rows = WJ // row_devices
    reduced_total = lax.psum(partial_value, "row")
    reduced_total = lax.dynamic_slice_in_dim(
        reduced_total, row_positions * shared_rows, shared_rows, 1
    )
    active_flags = active_columns.astype(jnp.float32)
    owned_active = lax.dynamic_slice_in_dim(
        active_flags, row_positions * shared_rows, shared_rows, 1
    )
    selected_diagonal_inverse = (
        (diagonal_inverse_blocks + reduced_total)
        * owned_active[:, :, None]
        * active_flags[:, None, :]
    )
    slot_live = jnp.sum(placed.astype(jnp.float32), axis=1)
    own_slots = lax.dynamic_slice_in_dim(slot_live, row_positions * own_blocks, own_blocks, 1)
    active_rows = jnp.repeat(own_slots.T, B, axis=0)
    selected_panel_inverse = -product_table * active_rows[:, :, None] * active_flags[None, :, :]
    return (selected_panel_inverse, selected_diagonal_inverse)


def solution(mesh):
    placed = (
        P("row", "snode"),
        P("snode", "row", None),
        P("snode", "row", None),
        P("snode", None),
        P("snode"),
        P("snode"),
        P(),
    )
    return jax.shard_map(
        body,
        mesh=mesh,
        in_specs=placed,
        out_specs=(P("row", "snode", None), P("snode", "row", None)),
        check_vma=False,
    )
```

```python
import jax
import jax.numpy as jnp
from jax import lax
from jax.sharding import PartitionSpec as P

B = 128
KMAX = 32
WJ = 128
NB = 64


def slot_table(block_list, block_count, child_width, owner_slot):
    block_ids = jnp.arange(NB, dtype=jnp.int32)
    named = block_list[:, :, None] == block_ids[None, None, :]
    slot_ids = jnp.sum(jnp.where(named, owner_slot[None, None, :], 0), axis=2)
    valid_blocks = jnp.arange(KMAX, dtype=jnp.int32)[None, :] < block_count[:, None]
    placed = (slot_ids[:, :, None] == block_ids[None, None, :]) & valid_blocks[:, :, None]
    active_columns = jnp.arange(WJ, dtype=jnp.int32)[None, :] < child_width[:, None]
    return (placed, active_columns)


def expand_rows(place_table, blocks):
    children = blocks.shape[0]
    spread = jnp.einsum("ckn,ckbj->nbcj", place_table, blocks, preferred_element_type=jnp.float32)
    return spread.astype(jnp.bfloat16).reshape(place_table.shape[2] * B, children * WJ)


def body(
    ancestor_sigma,
    child_panels,
    diagonal_inverse_blocks,
    block_list,
    block_count,
    child_width,
    owner_slot,
):
    row_devices = lax.axis_size("row")
    row_positions = lax.axis_index("row")
    children = child_panels.shape[0]
    local_rows = ancestor_sigma.shape[0]
    placed, active_columns = slot_table(block_list, block_count, child_width, owner_slot)
    place_bf = placed.astype(jnp.bfloat16)
    if row_devices == 2:
        partner = lax.ppermute(child_panels, "row", [(0, 1), (1, 0)])
        first = row_positions == 0
        gathered = jnp.concatenate(
            [jnp.where(first, child_panels, partner), jnp.where(first, partner, child_panels)], axis=1
        )
    else:
        gathered = lax.all_gather(child_panels, "row", axis=1, tiled=True)
    blocks = gathered.reshape(children, KMAX, B, WJ)
    blocks = jnp.where(active_columns[:, None, None, :], blocks, jnp.zeros_like(blocks))
    panel_rows = expand_rows(place_bf, blocks)
    product = jnp.dot(
        lax.all_gather(ancestor_sigma, "snode", axis=1, tiled=True),
        panel_rows,
        preferred_element_type=jnp.float32,
    )
    product_table = product.reshape(local_rows, children, WJ)
    own_blocks = local_rows // B
    own_table = lax.dynamic_slice_in_dim(place_bf, row_positions * own_blocks, own_blocks, 2)
    own_rows = expand_rows(own_table, blocks).reshape(local_rows, children, WJ)
    product_top = lax.reduce_precision(product_table, exponent_bits=8, mantissa_bits=7)
    product_hi = product_top.astype(jnp.bfloat16)
    product_lo = (product_table - product_top).astype(jnp.bfloat16)
    partial_value = jnp.einsum(
        "nca,ncb->cab", own_rows, product_hi, preferred_element_type=jnp.float32
    ) + jnp.einsum("nca,ncb->cab", own_rows, product_lo, preferred_element_type=jnp.float32)
    shared_rows = WJ // row_devices
    if row_devices == 2:
        reduced_total = partial_value + lax.ppermute(partial_value, "row", [(0, 1), (1, 0)])
    else:
        reduced_total = lax.psum(partial_value, "row")
    reduced_total = lax.dynamic_slice_in_dim(
        reduced_total, row_positions * shared_rows, shared_rows, 1
    )
    active_flags = active_columns.astype(jnp.float32)
    owned_active = lax.dynamic_slice_in_dim(
        active_flags, row_positions * shared_rows, shared_rows, 1
    )
    selected_diagonal_inverse = (
        (diagonal_inverse_blocks + reduced_total)
        * owned_active[:, :, None]
        * active_flags[:, None, :]
    )
    slot_live = jnp.sum(placed.astype(jnp.float32), axis=1)
    own_slots = lax.dynamic_slice_in_dim(slot_live, row_positions * own_blocks, own_blocks, 1)
    active_rows = jnp.repeat(own_slots.T, B, axis=0)
    selected_panel_inverse = -product_table * active_rows[:, :, None] * active_flags[None, :, :]
    return (selected_panel_inverse, selected_diagonal_inverse)


def solution(mesh):
    placed = (
        P("row", "snode"),
        P("snode", "row", None),
        P("snode", "row", None),
        P("snode", None),
        P("snode"),
        P("snode"),
        P(),
    )
    return jax.shard_map(
        body,
        mesh=mesh,
        in_specs=placed,
        out_specs=(P("row", "snode", None), P("snode", "row", None)),
        check_vma=False,
    )
```

```python
import jax
import jax.numpy as jnp
from jax import lax
from jax.sharding import PartitionSpec as P

B = 128
KMAX = 32
WJ = 128
NB = 64


def slot_table(block_list, block_count, child_width, owner_slot):
    block_ids = jnp.arange(NB, dtype=jnp.int32)
    named = block_list[:, :, None] == block_ids[None, None, :]
    slot_ids = jnp.sum(jnp.where(named, owner_slot[None, None, :], 0), axis=2)
    valid_blocks = jnp.arange(KMAX, dtype=jnp.int32)[None, :] < block_count[:, None]
    placed = (slot_ids[:, :, None] == block_ids[None, None, :]) & valid_blocks[:, :, None]
    active_columns = jnp.arange(WJ, dtype=jnp.int32)[None, :] < child_width[:, None]
    return (placed, active_columns)


def expand_rows(place_table, blocks):
    children = blocks.shape[0]
    spread = jnp.einsum("ckn,ckbj->nbcj", place_table, blocks, preferred_element_type=jnp.float32)
    return spread.astype(jnp.bfloat16).reshape(place_table.shape[2] * B, children * WJ)


def body(
    ancestor_sigma,
    child_panels,
    diagonal_inverse_blocks,
    block_list,
    block_count,
    child_width,
    owner_slot,
):
    row_devices = lax.axis_size("row")
    row_positions = lax.axis_index("row")
    children = child_panels.shape[0]
    local_rows = ancestor_sigma.shape[0]
    placed, active_columns = slot_table(block_list, block_count, child_width, owner_slot)
    place_bf = placed.astype(jnp.bfloat16)
    if row_devices == 2:
        partner = lax.ppermute(child_panels, "row", [(0, 1), (1, 0)])
        first = row_positions == 0
        gathered = jnp.concatenate(
            [jnp.where(first, child_panels, partner), jnp.where(first, partner, child_panels)], axis=1
        )
    else:
        gathered = lax.all_gather(child_panels, "row", axis=1, tiled=True)
    blocks = gathered.reshape(children, KMAX, B, WJ)
    blocks = jnp.where(active_columns[:, None, None, :], blocks, jnp.zeros_like(blocks))
    panel_rows = expand_rows(place_bf, blocks)
    flipped = lax.all_gather(ancestor_sigma.T, "snode", axis=0, tiled=True)
    product = lax.dot_general(
        flipped, panel_rows, (((0,), (0,)), ((), ())), preferred_element_type=jnp.float32
    )
    product_table = product.reshape(local_rows, children, WJ)
    own_blocks = local_rows // B
    own_table = lax.dynamic_slice_in_dim(place_bf, row_positions * own_blocks, own_blocks, 2)
    own_rows = expand_rows(own_table, blocks).reshape(local_rows, children, WJ)
    partial_value = jnp.einsum(
        "nca,ncb->cab", own_rows.astype(jnp.float32), product_table, precision=lax.Precision.HIGHEST
    )
    shared_rows = WJ // row_devices
    if row_devices == 2:
        reduced_total = partial_value + lax.ppermute(partial_value, "row", [(0, 1), (1, 0)])
    else:
        reduced_total = lax.psum(partial_value, "row")
    reduced_total = lax.dynamic_slice_in_dim(
        reduced_total, row_positions * shared_rows, shared_rows, 1
    )
    active_flags = active_columns.astype(jnp.float32)
    owned_active = lax.dynamic_slice_in_dim(
        active_flags, row_positions * shared_rows, shared_rows, 1
    )
    selected_diagonal_inverse = (
        (diagonal_inverse_blocks + reduced_total)
        * owned_active[:, :, None]
        * active_flags[:, None, :]
    )
    slot_live = jnp.sum(placed.astype(jnp.float32), axis=1)
    own_slots = lax.dynamic_slice_in_dim(slot_live, row_positions * own_blocks, own_blocks, 1)
    active_rows = jnp.repeat(own_slots.T, B, axis=0)
    selected_panel_inverse = -product_table * active_rows[:, :, None] * active_flags[None, :, :]
    return (selected_panel_inverse, selected_diagonal_inverse)


def solution(mesh):
    placed = (
        P("row", "snode"),
        P("snode", "row", None),
        P("snode", "row", None),
        P("snode", None),
        P("snode"),
        P("snode"),
        P(),
    )
    return jax.shard_map(
        body,
        mesh=mesh,
        in_specs=placed,
        out_specs=(P("row", "snode", None), P("snode", "row", None)),
        check_vma=False,
    )
```

```python
import numpy as np
import jax
import jax.numpy as jnp
from jax import lax
from jax.sharding import PartitionSpec as P

B = 128
KMAX = 32
WJ = 128
NB = 64


def slot_table(block_list, block_count, child_width, owner_slot):
    block_ids = jnp.arange(NB, dtype=jnp.int32)
    named = block_list[:, :, None] == block_ids[None, None, :]
    slot_ids = jnp.sum(jnp.where(named, owner_slot[None, None, :], 0), axis=2)
    valid_blocks = jnp.arange(KMAX, dtype=jnp.int32)[None, :] < block_count[:, None]
    placed = (slot_ids[:, :, None] == block_ids[None, None, :]) & valid_blocks[:, :, None]
    active_columns = jnp.arange(WJ, dtype=jnp.int32)[None, :] < child_width[:, None]
    return (placed, active_columns)


def expand_rows(place_table, blocks):
    children = blocks.shape[0]
    spread = jnp.einsum("ckn,ckbj->nbcj", place_table, blocks, preferred_element_type=jnp.float32)
    return spread.astype(jnp.bfloat16).reshape(place_table.shape[2] * B, children * WJ)


def symmetric_rows(ancestor_sigma, row_position, snode_position, snode_devices):
    width = ancestor_sigma.shape[1]
    half = snode_devices // 2
    quarter = half // 2
    blocks = ancestor_sigma.reshape(half, width, width)
    chip_local = snode_position % half
    shift = jnp.where(snode_position // half == row_position, 0, row_position)
    pick = (chip_local + shift + jnp.arange(quarter + 1)) % half
    gathered = lax.all_gather(jnp.take(blocks, pick, axis=0), "snode", axis=0)
    own = lax.dynamic_slice_in_dim(gathered, row_position * half, half, 0)
    other = lax.dynamic_slice_in_dim(gathered, (1 - row_position) * half, half, 0)
    partner = lax.ppermute(other[:, :quarter], "row", [(0, 1), (1, 0)])

    u = np.arange(half)[:, None] + np.zeros((1, half), np.int64)
    t = np.arange(half)[None, :] + np.zeros((half, 1), np.int64)
    d = (u - t) % half
    direct = d <= quarter
    near = own[np.where(direct, t, u), np.where(direct, d, half - d)]
    near = jnp.where(direct[:, :, None, None], near, jnp.swapaxes(near, -1, -2))
    near = near.transpose(0, 2, 1, 3).reshape(half * width, half * width)

    e = (u - t - row_position) % half
    straight = e < quarter
    far_a = other[t, jnp.where(straight, e, 0)]
    far_b = partner[u, jnp.where(straight, 0, half - 1 - e)]
    far = jnp.where(straight[:, :, None, None], far_a, jnp.swapaxes(far_b, -1, -2))
    far = far.transpose(0, 2, 1, 3).reshape(half * width, half * width)
    return near, far


def body(
    ancestor_sigma,
    child_panels,
    diagonal_inverse_blocks,
    block_list,
    block_count,
    child_width,
    owner_slot,
):
    row_devices = lax.axis_size("row")
    row_positions = lax.axis_index("row")
    children = child_panels.shape[0]
    local_rows = ancestor_sigma.shape[0]
    placed, active_columns = slot_table(block_list, block_count, child_width, owner_slot)
    place_bf = placed.astype(jnp.bfloat16)
    if row_devices == 2:
        partner = lax.ppermute(child_panels, "row", [(0, 1), (1, 0)])
        first = row_positions == 0
        gathered = jnp.concatenate(
            [jnp.where(first, child_panels, partner), jnp.where(first, partner, child_panels)], axis=1
        )
    else:
        gathered = lax.all_gather(child_panels, "row", axis=1, tiled=True)
    blocks = gathered.reshape(children, KMAX, B, WJ)
    blocks = jnp.where(active_columns[:, None, None, :], blocks, jnp.zeros_like(blocks))
    panel_rows = expand_rows(place_bf, blocks)
    snode_devices = lax.axis_size("snode")
    width = ancestor_sigma.shape[1]
    if row_devices == 2 and snode_devices % 4 == 0 and local_rows == width * snode_devices // 2:
        near, far = symmetric_rows(
            ancestor_sigma, row_positions, lax.axis_index("snode"), snode_devices
        )
        product = jnp.dot(
            near,
            lax.dynamic_slice_in_dim(panel_rows, row_positions * local_rows, local_rows, 0),
            preferred_element_type=jnp.float32,
        ) + jnp.dot(
            far,
            lax.dynamic_slice_in_dim(panel_rows, (1 - row_positions) * local_rows, local_rows, 0),
            preferred_element_type=jnp.float32,
        )
    else:
        flipped = lax.all_gather(ancestor_sigma.T, "snode", axis=0, tiled=True)
        product = lax.dot_general(
            flipped, panel_rows, (((0,), (0,)), ((), ())), preferred_element_type=jnp.float32
        )
    product_table = product.reshape(local_rows, children, WJ)
    own_blocks = local_rows // B
    own_table = lax.dynamic_slice_in_dim(place_bf, row_positions * own_blocks, own_blocks, 2)
    own_rows = expand_rows(own_table, blocks).reshape(local_rows, children, WJ)
    partial_value = jnp.einsum(
        "nca,ncb->cab", own_rows.astype(jnp.float32), product_table, precision=lax.Precision.HIGHEST
    )
    shared_rows = WJ // row_devices
    if row_devices == 2:
        reduced_total = partial_value + lax.ppermute(partial_value, "row", [(0, 1), (1, 0)])
    else:
        reduced_total = lax.psum(partial_value, "row")
    reduced_total = lax.dynamic_slice_in_dim(
        reduced_total, row_positions * shared_rows, shared_rows, 1
    )
    active_flags = active_columns.astype(jnp.float32)
    owned_active = lax.dynamic_slice_in_dim(
        active_flags, row_positions * shared_rows, shared_rows, 1
    )
    selected_diagonal_inverse = (
        (diagonal_inverse_blocks + reduced_total)
        * owned_active[:, :, None]
        * active_flags[:, None, :]
    )
    slot_live = jnp.sum(placed.astype(jnp.float32), axis=1)
    own_slots = lax.dynamic_slice_in_dim(slot_live, row_positions * own_blocks, own_blocks, 1)
    active_rows = jnp.repeat(own_slots.T, B, axis=0)
    selected_panel_inverse = -product_table * active_rows[:, :, None] * active_flags[None, :, :]
    return (selected_panel_inverse, selected_diagonal_inverse)


def solution(mesh):
    placed = (
        P("row", "snode"),
        P("snode", "row", None),
        P("snode", "row", None),
        P("snode", None),
        P("snode"),
        P("snode"),
        P(),
    )
    return jax.shard_map(
        body,
        mesh=mesh,
        in_specs=placed,
        out_specs=(P("row", "snode", None), P("snode", "row", None)),
        check_vma=False,
    )
```

```python
import numpy as np
import jax
import jax.numpy as jnp
from jax import lax
from jax.experimental import pallas as pl
from jax.experimental.pallas import tpu as pltpu
from jax.sharding import PartitionSpec as P

B = 128
KMAX = 32
WJ = 128
NB = 64


def slot_table(block_list, block_count, child_width, owner_slot):
    block_ids = jnp.arange(NB, dtype=jnp.int32)
    named = block_list[:, :, None] == block_ids[None, None, :]
    slot_ids = jnp.sum(jnp.where(named, owner_slot[None, None, :], 0), axis=2)
    valid_blocks = jnp.arange(KMAX, dtype=jnp.int32)[None, :] < block_count[:, None]
    placed = (slot_ids[:, :, None] == block_ids[None, None, :]) & valid_blocks[:, :, None]
    active_columns = jnp.arange(WJ, dtype=jnp.int32)[None, :] < child_width[:, None]
    return (placed, active_columns)


def expand_rows(place_table, blocks):
    children = blocks.shape[0]
    spread = jnp.einsum("ckn,ckbj->nbcj", place_table, blocks, preferred_element_type=jnp.float32)
    return spread.astype(jnp.bfloat16).reshape(place_table.shape[2] * B, children * WJ)


def block_product_kernel(src_ref, far_ref, pick_ref, flip_ref, pool_ref, swap_ref, rows_ref, out_ref, acc_ref):
    t = pl.program_id(1)
    at = pl.program_id(0) * pl.num_programs(1) + t

    @pl.when(t == 0)
    def _():
        acc_ref[...] = jnp.zeros_like(acc_ref)

    block = jnp.where(pick_ref[at] == 0, pool_ref[0], swap_ref[0])
    block = lax.cond(flip_ref[at] == 1, lambda b: b.T, lambda b: b, block)
    acc_ref[...] += jnp.dot(block, rows_ref[0], preferred_element_type=jnp.float32)

    @pl.when(t == pl.num_programs(1) - 1)
    def _():
        out_ref[...] = acc_ref[...]


def symmetric_product(ancestor_sigma, panel_rows, row_position, snode_position, snode_devices):
    width = ancestor_sigma.shape[1]
    half = snode_devices // 2
    quarter = half // 2
    cols = panel_rows.shape[1]
    blocks = ancestor_sigma.reshape(half, width, width)
    chip_local = snode_position % half
    shift = jnp.where(snode_position // half == row_position, 0, row_position)
    pick = (chip_local + shift + jnp.arange(quarter + 1)) % half
    gathered = lax.all_gather(jnp.take(blocks, pick, axis=0), "snode", axis=0)
    other = lax.dynamic_slice_in_dim(gathered, (1 - row_position) * half, half, 0)
    partner = lax.ppermute(other[:, :quarter], "row", [(0, 1), (1, 0)])
    pool = gathered.reshape(snode_devices * (quarter + 1), width, width)
    swap = partner.reshape(half * quarter, width, width)

    u = jnp.arange(half)[:, None]
    t = jnp.arange(snode_devices)[None, :]
    near = (t // half) == row_position
    local = t % half
    d = (u - local) % half
    near_src = jnp.where(
        d <= quarter,
        (row_position * half + local) * (quarter + 1) + d,
        (row_position * half + u) * (quarter + 1) + half - d,
    )
    e = (u - local - row_position) % half
    straight = e < quarter
    far_src = ((1 - row_position) * half + local) * (quarter + 1) + jnp.where(straight, e, 0)
    src = jnp.where(near, near_src, jnp.where(straight, far_src, 0))
    far = jnp.where(near | straight, 0, u * quarter + half - 1 - e)
    pick_swap = jnp.where(near | straight, 0, 1)
    flip = jnp.where(near, d > quarter, ~straight).astype(jnp.int32)
    tables = [x.reshape(-1).astype(jnp.int32) for x in (src, far, pick_swap, flip)]

    grid_spec = pltpu.PrefetchScalarGridSpec(
        num_scalar_prefetch=4,
        grid=(half, snode_devices),
        in_specs=[
            pl.BlockSpec((1, width, width), lambda i, j, s, f, p, q: (s[i * snode_devices + j], 0, 0)),
            pl.BlockSpec((1, width, width), lambda i, j, s, f, p, q: (f[i * snode_devices + j], 0, 0)),
            pl.BlockSpec((1, width, cols), lambda i, j, s, f, p, q: (j, 0, 0)),
        ],
        out_specs=pl.BlockSpec((width, cols), lambda i, j, s, f, p, q: (i, 0)),
        scratch_shapes=[pltpu.VMEM((width, cols), jnp.float32)],
    )
    return pl.pallas_call(
        block_product_kernel,
        grid_spec=grid_spec,
        out_shape=jax.ShapeDtypeStruct((half * width, cols), jnp.float32),
    )(*tables, pool, swap, panel_rows.reshape(snode_devices, width, cols))

def body(
    ancestor_sigma,
    child_panels,
    diagonal_inverse_blocks,
    block_list,
    block_count,
    child_width,
    owner_slot,
):
    row_devices = lax.axis_size("row")
    row_positions = lax.axis_index("row")
    children = child_panels.shape[0]
    local_rows = ancestor_sigma.shape[0]
    placed, active_columns = slot_table(block_list, block_count, child_width, owner_slot)
    place_bf = placed.astype(jnp.bfloat16)
    if row_devices == 2:
        partner = lax.ppermute(child_panels, "row", [(0, 1), (1, 0)])
        first = row_positions == 0
        gathered = jnp.concatenate(
            [jnp.where(first, child_panels, partner), jnp.where(first, partner, child_panels)], axis=1
        )
    else:
        gathered = lax.all_gather(child_panels, "row", axis=1, tiled=True)
    blocks = gathered.reshape(children, KMAX, B, WJ)
    blocks = jnp.where(active_columns[:, None, None, :], blocks, jnp.zeros_like(blocks))
    panel_rows = expand_rows(place_bf, blocks)
    snode_devices = lax.axis_size("snode")
    width = ancestor_sigma.shape[1]
    if row_devices == 2 and snode_devices % 4 == 0 and local_rows == width * snode_devices // 2:
        product = symmetric_product(
            ancestor_sigma, panel_rows, row_positions, lax.axis_index("snode"), snode_devices
        )
    else:
        flipped = lax.all_gather(ancestor_sigma.T, "snode", axis=0, tiled=True)
        product = lax.dot_general(
            flipped, panel_rows, (((0,), (0,)), ((), ())), preferred_element_type=jnp.float32
        )
    product_table = product.reshape(local_rows, children, WJ)
    own_blocks = local_rows // B
    own_table = lax.dynamic_slice_in_dim(place_bf, row_positions * own_blocks, own_blocks, 2)
    own_rows = expand_rows(own_table, blocks).reshape(local_rows, children, WJ)
    partial_value = jnp.einsum(
        "nca,ncb->cab", own_rows.astype(jnp.float32), product_table, precision=lax.Precision.HIGHEST
    )
    shared_rows = WJ // row_devices
    if row_devices == 2:
        reduced_total = partial_value + lax.ppermute(partial_value, "row", [(0, 1), (1, 0)])
    else:
        reduced_total = lax.psum(partial_value, "row")
    reduced_total = lax.dynamic_slice_in_dim(
        reduced_total, row_positions * shared_rows, shared_rows, 1
    )
    active_flags = active_columns.astype(jnp.float32)
    owned_active = lax.dynamic_slice_in_dim(
        active_flags, row_positions * shared_rows, shared_rows, 1
    )
    selected_diagonal_inverse = (
        (diagonal_inverse_blocks + reduced_total)
        * owned_active[:, :, None]
        * active_flags[:, None, :]
    )
    slot_live = jnp.sum(placed.astype(jnp.float32), axis=1)
    own_slots = lax.dynamic_slice_in_dim(slot_live, row_positions * own_blocks, own_blocks, 1)
    active_rows = jnp.repeat(own_slots.T, B, axis=0)
    selected_panel_inverse = -product_table * active_rows[:, :, None] * active_flags[None, :, :]
    return (selected_panel_inverse, selected_diagonal_inverse)


def solution(mesh):
    placed = (
        P("row", "snode"),
        P("snode", "row", None),
        P("snode", "row", None),
        P("snode", None),
        P("snode"),
        P("snode"),
        P(),
    )
    return jax.shard_map(
        body,
        mesh=mesh,
        in_specs=placed,
        out_specs=(P("row", "snode", None), P("snode", "row", None)),
        check_vma=False,
    )
```

```python
import numpy as np
import jax
import jax.numpy as jnp
from jax import lax
from jax.experimental import pallas as pl
from jax.experimental.pallas import tpu as pltpu
from jax.sharding import PartitionSpec as P

B = 128
KMAX = 32
WJ = 128
NB = 64


def slot_table(block_list, block_count, child_width, owner_slot):
    block_ids = jnp.arange(NB, dtype=jnp.int32)
    named = block_list[:, :, None] == block_ids[None, None, :]
    slot_ids = jnp.sum(jnp.where(named, owner_slot[None, None, :], 0), axis=2)
    valid_blocks = jnp.arange(KMAX, dtype=jnp.int32)[None, :] < block_count[:, None]
    placed = (slot_ids[:, :, None] == block_ids[None, None, :]) & valid_blocks[:, :, None]
    active_columns = jnp.arange(WJ, dtype=jnp.int32)[None, :] < child_width[:, None]
    return (placed, active_columns)


def expand_rows(place_table, blocks):
    children = blocks.shape[0]
    spread = jnp.einsum("ckn,ckbj->nbcj", place_table, blocks, preferred_element_type=jnp.float32)
    return spread.astype(jnp.bfloat16).reshape(place_table.shape[2] * B, children * WJ)


def block_product_kernel(src_ref, far_ref, pick_ref, flip_ref, pool_ref, swap_ref, rows_ref, out_ref):
    t = pl.program_id(0)
    u = pl.program_id(1)
    at = u * pl.num_programs(0) + t
    width = pool_ref.shape[1]
    block = jnp.where(pick_ref[at] == 0, pool_ref[0], swap_ref[0])
    block = lax.cond(flip_ref[at] == 1, lambda b: b.T, lambda b: b, block)
    contrib = jnp.dot(block, rows_ref[0], preferred_element_type=jnp.float32)
    rows = pl.ds(pl.multiple_of(u * width, width), width)

    @pl.when(t == 0)
    def _():
        out_ref[rows, :] = contrib

    @pl.when(t > 0)
    def _():
        out_ref[rows, :] += contrib


def symmetric_product(ancestor_sigma, panel_rows, row_position, snode_position, snode_devices):
    width = ancestor_sigma.shape[1]
    half = snode_devices // 2
    quarter = half // 2
    cols = panel_rows.shape[1]
    blocks = ancestor_sigma.reshape(half, width, width)
    chip_local = snode_position % half
    shift = jnp.where(snode_position // half == row_position, 0, row_position)
    pick = (chip_local + shift + jnp.arange(quarter + 1)) % half
    gathered = lax.all_gather(jnp.take(blocks, pick, axis=0), "snode", axis=0)
    other = lax.dynamic_slice_in_dim(gathered, (1 - row_position) * half, half, 0)
    partner = lax.ppermute(other[:, :quarter], "row", [(0, 1), (1, 0)])
    pool = gathered.reshape(snode_devices * (quarter + 1), width, width)
    swap = partner.reshape(half * quarter, width, width)

    u = jnp.arange(half)[:, None]
    t = jnp.arange(snode_devices)[None, :]
    near = (t // half) == row_position
    local = t % half
    d = (u - local) % half
    near_src = jnp.where(
        d <= quarter,
        (row_position * half + local) * (quarter + 1) + d,
        (row_position * half + u) * (quarter + 1) + half - d,
    )
    e = (u - local - row_position) % half
    straight = e < quarter
    far_src = ((1 - row_position) * half + local) * (quarter + 1) + jnp.where(straight, e, 0)
    src = jnp.where(near, near_src, jnp.where(straight, far_src, 0))
    far = jnp.where(near | straight, 0, u * quarter + half - 1 - e)
    pick_swap = jnp.where(near | straight, 0, 1)
    flip = jnp.where(near, d > quarter, ~straight).astype(jnp.int32)
    tables = [x.reshape(-1).astype(jnp.int32) for x in (src, far, pick_swap, flip)]

    grid_spec = pltpu.PrefetchScalarGridSpec(
        num_scalar_prefetch=4,
        grid=(snode_devices, half),
        in_specs=[
            pl.BlockSpec((1, width, width), lambda j, i, s, f, p, q: (s[i * snode_devices + j], 0, 0)),
            pl.BlockSpec((1, width, width), lambda j, i, s, f, p, q: (f[i * snode_devices + j], 0, 0)),
            pl.BlockSpec((1, width, cols), lambda j, i, s, f, p, q: (j, 0, 0)),
        ],
        out_specs=pl.BlockSpec((half * width, cols), lambda j, i, s, f, p, q: (0, 0)),
    )
    return pl.pallas_call(
        block_product_kernel,
        grid_spec=grid_spec,
        out_shape=jax.ShapeDtypeStruct((half * width, cols), jnp.float32),
    )(*tables, pool, swap, panel_rows.reshape(snode_devices, width, cols))

def body(
    ancestor_sigma,
    child_panels,
    diagonal_inverse_blocks,
    block_list,
    block_count,
    child_width,
    owner_slot,
):
    row_devices = lax.axis_size("row")
    row_positions = lax.axis_index("row")
    children = child_panels.shape[0]
    local_rows = ancestor_sigma.shape[0]
    placed, active_columns = slot_table(block_list, block_count, child_width, owner_slot)
    place_bf = placed.astype(jnp.bfloat16)
    if row_devices == 2:
        partner = lax.ppermute(child_panels, "row", [(0, 1), (1, 0)])
        ancestor_sigma, partner = lax.optimization_barrier((ancestor_sigma, partner))
        first = row_positions == 0
        gathered = jnp.concatenate(
            [jnp.where(first, child_panels, partner), jnp.where(first, partner, child_panels)], axis=1
        )
    else:
        gathered = lax.all_gather(child_panels, "row", axis=1, tiled=True)
    blocks = gathered.reshape(children, KMAX, B, WJ)
    blocks = jnp.where(active_columns[:, None, None, :], blocks, jnp.zeros_like(blocks))
    panel_rows = expand_rows(place_bf, blocks)
    snode_devices = lax.axis_size("snode")
    width = ancestor_sigma.shape[1]
    if row_devices == 2 and snode_devices % 4 == 0 and local_rows == width * snode_devices // 2:
        product = symmetric_product(
            ancestor_sigma, panel_rows, row_positions, lax.axis_index("snode"), snode_devices
        )
    else:
        flipped = lax.all_gather(ancestor_sigma.T, "snode", axis=0, tiled=True)
        product = lax.dot_general(
            flipped, panel_rows, (((0,), (0,)), ((), ())), preferred_element_type=jnp.float32
        )
    product_table = product.reshape(local_rows, children, WJ)
    own_blocks = local_rows // B
    own_table = lax.dynamic_slice_in_dim(place_bf, row_positions * own_blocks, own_blocks, 2)
    own_rows = expand_rows(own_table, blocks).reshape(local_rows, children, WJ)
    partial_value = jnp.einsum(
        "nca,ncb->cab", own_rows.astype(jnp.float32), product_table, precision=lax.Precision.HIGHEST
    )
    shared_rows = WJ // row_devices
    if row_devices == 2:
        reduced_total = partial_value + lax.ppermute(partial_value, "row", [(0, 1), (1, 0)])
    else:
        reduced_total = lax.psum(partial_value, "row")
    reduced_total = lax.dynamic_slice_in_dim(
        reduced_total, row_positions * shared_rows, shared_rows, 1
    )
    active_flags = active_columns.astype(jnp.float32)
    owned_active = lax.dynamic_slice_in_dim(
        active_flags, row_positions * shared_rows, shared_rows, 1
    )
    selected_diagonal_inverse = (
        (diagonal_inverse_blocks + reduced_total)
        * owned_active[:, :, None]
        * active_flags[:, None, :]
    )
    slot_live = jnp.sum(placed.astype(jnp.float32), axis=1)
    own_slots = lax.dynamic_slice_in_dim(slot_live, row_positions * own_blocks, own_blocks, 1)
    active_rows = jnp.repeat(own_slots.T, B, axis=0)
    selected_panel_inverse = -product_table * active_rows[:, :, None] * active_flags[None, :, :]
    return (selected_panel_inverse, selected_diagonal_inverse)


def solution(mesh):
    placed = (
        P("row", "snode"),
        P("snode", "row", None),
        P("snode", "row", None),
        P("snode", None),
        P("snode"),
        P("snode"),
        P(),
    )
    return jax.shard_map(
        body,
        mesh=mesh,
        in_specs=placed,
        out_specs=(P("row", "snode", None), P("snode", "row", None)),
        check_vma=False,
    )
```

```python
import numpy as np
import jax
import jax.numpy as jnp
from jax import lax
from jax.experimental import pallas as pl
from jax.experimental.pallas import tpu as pltpu
from jax.sharding import PartitionSpec as P

B = 128
KMAX = 32
WJ = 128
NB = 64


def slot_table(block_list, block_count, child_width, owner_slot):
    block_ids = jnp.arange(NB, dtype=jnp.int32)
    named = block_list[:, :, None] == block_ids[None, None, :]
    slot_ids = jnp.sum(jnp.where(named, owner_slot[None, None, :], 0), axis=2)
    valid_blocks = jnp.arange(KMAX, dtype=jnp.int32)[None, :] < block_count[:, None]
    placed = (slot_ids[:, :, None] == block_ids[None, None, :]) & valid_blocks[:, :, None]
    active_columns = jnp.arange(WJ, dtype=jnp.int32)[None, :] < child_width[:, None]
    return (placed, active_columns)


def expand_rows(place_table, blocks):
    children = blocks.shape[0]
    spread = jnp.einsum("ckn,ckbj->nbcj", place_table, blocks, preferred_element_type=jnp.float32)
    return spread.astype(jnp.bfloat16).reshape(place_table.shape[2] * B, children * WJ)


def block_product_kernel(src_ref, far_ref, pick_ref, flip_ref, pool_ref, swap_ref, rows_ref, out_ref):
    t = pl.program_id(0)
    u = pl.program_id(1)
    at = u * pl.num_programs(0) + t
    width = pool_ref.shape[1]
    block = jnp.where(pick_ref[at] == 0, pool_ref[0], swap_ref[0])
    block = lax.cond(flip_ref[at] == 1, lambda b: b.T, lambda b: b, block)
    contrib = jnp.dot(block, rows_ref[0], preferred_element_type=jnp.float32)
    rows = pl.ds(pl.multiple_of(u * width, width), width)

    @pl.when(t == 0)
    def _():
        out_ref[rows, :] = contrib

    @pl.when(t > 0)
    def _():
        out_ref[rows, :] += contrib


def symmetric_product(ancestor_sigma, panel_rows, row_position, snode_position, snode_devices):
    width = ancestor_sigma.shape[1]
    half = snode_devices // 2
    quarter = half // 2
    cols = panel_rows.shape[1]
    blocks = ancestor_sigma.reshape(half, width, width)
    chip_local = snode_position % half
    shift = jnp.where(snode_position // half == row_position, 0, row_position)
    pick = (chip_local + shift + jnp.arange(quarter + 1)) % half
    gathered = lax.all_gather(jnp.take(blocks, pick, axis=0), "snode", axis=0)
    other = lax.dynamic_slice_in_dim(gathered, (1 - row_position) * half, half, 0)
    partner = lax.ppermute(other[:, :quarter], "row", [(0, 1), (1, 0)])
    pool = gathered.reshape(snode_devices * (quarter + 1), width, width)
    swap = partner.reshape(half * quarter, width, width)

    u = jnp.arange(half)[:, None]
    t = jnp.arange(snode_devices)[None, :]
    near = (t // half) == row_position
    local = t % half
    d = (u - local) % half
    near_src = jnp.where(
        d <= quarter,
        (row_position * half + local) * (quarter + 1) + d,
        (row_position * half + u) * (quarter + 1) + half - d,
    )
    e = (u - local - row_position) % half
    straight = e < quarter
    far_src = ((1 - row_position) * half + local) * (quarter + 1) + jnp.where(straight, e, 0)
    src = jnp.where(near, near_src, jnp.where(straight, far_src, 0))
    far = jnp.where(near | straight, 0, u * quarter + half - 1 - e)
    pick_swap = jnp.where(near | straight, 0, 1)
    flip = jnp.where(near, d > quarter, ~straight).astype(jnp.int32)
    tables = [x.reshape(-1).astype(jnp.int32) for x in (src, far, pick_swap, flip)]

    grid_spec = pltpu.PrefetchScalarGridSpec(
        num_scalar_prefetch=4,
        grid=(snode_devices, half),
        in_specs=[
            pl.BlockSpec((1, width, width), lambda j, i, s, f, p, q: (s[i * snode_devices + j], 0, 0)),
            pl.BlockSpec((1, width, width), lambda j, i, s, f, p, q: (f[i * snode_devices + j], 0, 0)),
            pl.BlockSpec((1, width, cols), lambda j, i, s, f, p, q: (j, 0, 0)),
        ],
        out_specs=pl.BlockSpec((half * width, cols), lambda j, i, s, f, p, q: (0, 0)),
    )
    return pl.pallas_call(
        block_product_kernel,
        grid_spec=grid_spec,
        out_shape=jax.ShapeDtypeStruct((half * width, cols), jnp.float32),
    )(*tables, pool, swap, panel_rows.reshape(snode_devices, width, cols))

def body(
    ancestor_sigma,
    child_panels,
    diagonal_inverse_blocks,
    block_list,
    block_count,
    child_width,
    owner_slot,
):
    row_devices = lax.axis_size("row")
    row_positions = lax.axis_index("row")
    children = child_panels.shape[0]
    local_rows = ancestor_sigma.shape[0]
    placed, active_columns = slot_table(block_list, block_count, child_width, owner_slot)
    place_bf = placed.astype(jnp.bfloat16)
    if row_devices == 2:
        partner = lax.ppermute(child_panels, "row", [(0, 1), (1, 0)])
        first = row_positions == 0
        gathered = jnp.concatenate(
            [jnp.where(first, child_panels, partner), jnp.where(first, partner, child_panels)], axis=1
        )
    else:
        gathered = lax.all_gather(child_panels, "row", axis=1, tiled=True)
    blocks = gathered.reshape(children, KMAX, B, WJ)
    blocks = jnp.where(active_columns[:, None, None, :], blocks, jnp.zeros_like(blocks))
    panel_rows = expand_rows(place_bf, blocks)
    snode_devices = lax.axis_size("snode")
    width = ancestor_sigma.shape[1]
    if row_devices == 2 and snode_devices % 4 == 0 and local_rows == width * snode_devices // 2:
        product = symmetric_product(
            ancestor_sigma, panel_rows, row_positions, lax.axis_index("snode"), snode_devices
        )
    else:
        flipped = lax.all_gather(ancestor_sigma.T, "snode", axis=0, tiled=True)
        product = lax.dot_general(
            flipped, panel_rows, (((0,), (0,)), ((), ())), preferred_element_type=jnp.float32
        )
    product_table = product.reshape(local_rows, children, WJ)
    own_blocks = local_rows // B
    own_table = lax.dynamic_slice_in_dim(place_bf, row_positions * own_blocks, own_blocks, 2)
    own_rows = expand_rows(own_table, blocks).reshape(local_rows, children, WJ)
    partial_value = jnp.einsum(
        "nca,ncb->cab", own_rows.astype(jnp.float32), product_table, precision=lax.Precision.HIGHEST
    )
    shared_rows = WJ // row_devices
    if row_devices == 2:
        reduced_total = partial_value + lax.ppermute(partial_value, "row", [(0, 1), (1, 0)])
    else:
        reduced_total = lax.psum(partial_value, "row")
    reduced_total = lax.dynamic_slice_in_dim(
        reduced_total, row_positions * shared_rows, shared_rows, 1
    )
    active_flags = active_columns.astype(jnp.float32)
    owned_active = lax.dynamic_slice_in_dim(
        active_flags, row_positions * shared_rows, shared_rows, 1
    )
    selected_diagonal_inverse = (
        (diagonal_inverse_blocks + reduced_total)
        * owned_active[:, :, None]
        * active_flags[:, None, :]
    )
    slot_live = jnp.sum(placed.astype(jnp.float32), axis=1)
    own_slots = lax.dynamic_slice_in_dim(slot_live, row_positions * own_blocks, own_blocks, 1)
    active_rows = jnp.repeat(own_slots.T, B, axis=0)
    selected_panel_inverse = -product_table * active_rows[:, :, None] * active_flags[None, :, :]
    return (selected_panel_inverse, selected_diagonal_inverse)


def solution(mesh):
    placed = (
        P("row", "snode"),
        P("snode", "row", None),
        P("snode", "row", None),
        P("snode", None),
        P("snode"),
        P("snode"),
        P(),
    )
    return jax.shard_map(
        body,
        mesh=mesh,
        in_specs=placed,
        out_specs=(P("row", "snode", None), P("snode", "row", None)),
        check_vma=False,
    )
```

```python
import numpy as np
import jax
import jax.numpy as jnp
from jax import lax
from jax.experimental import pallas as pl
from jax.experimental.pallas import tpu as pltpu
from jax.sharding import PartitionSpec as P

B = 128
KMAX = 32
WJ = 128
NB = 64


def slot_table(block_list, block_count, child_width, owner_slot):
    block_ids = jnp.arange(NB, dtype=jnp.int32)
    named = block_list[:, :, None] == block_ids[None, None, :]
    slot_ids = jnp.sum(jnp.where(named, owner_slot[None, None, :], 0), axis=2)
    valid_blocks = jnp.arange(KMAX, dtype=jnp.int32)[None, :] < block_count[:, None]
    placed = (slot_ids[:, :, None] == block_ids[None, None, :]) & valid_blocks[:, :, None]
    active_columns = jnp.arange(WJ, dtype=jnp.int32)[None, :] < child_width[:, None]
    return (placed, active_columns)


def expand_rows(place_table, blocks):
    children = blocks.shape[0]
    spread = jnp.einsum("ckn,ckbj->nbcj", place_table, blocks, preferred_element_type=jnp.float32)
    return spread.astype(jnp.bfloat16).reshape(place_table.shape[2] * B, children * WJ)


def block_product_kernel(src_ref, far_ref, pick_ref, flip_ref, pool_ref, swap_ref, rows_ref, out_ref):
    t = pl.program_id(0)
    u = pl.program_id(1)
    at = u * pl.num_programs(0) + t
    width = pool_ref.shape[1]
    def product_of(block):
        return jnp.dot(block, rows_ref[0], preferred_element_type=jnp.float32)

    contrib = lax.cond(
        pick_ref[at] == 0,
        lambda: lax.cond(
            flip_ref[at] == 1,
            lambda: product_of(pool_ref[0].T),
            lambda: product_of(pool_ref[0]),
        ),
        lambda: product_of(swap_ref[0].T),
    )
    rows = pl.ds(pl.multiple_of(u * width, width), width)

    @pl.when(t == 0)
    def _():
        out_ref[rows, :] = contrib

    @pl.when(t > 0)
    def _():
        out_ref[rows, :] += contrib


def symmetric_product(ancestor_sigma, panel_rows, row_position, snode_position, snode_devices):
    width = ancestor_sigma.shape[1]
    half = snode_devices // 2
    quarter = half // 2
    cols = panel_rows.shape[1]
    blocks = ancestor_sigma.reshape(half, width, width)
    chip_local = snode_position % half
    shift = jnp.where(snode_position // half == row_position, 0, row_position)
    pick = (chip_local + shift + jnp.arange(quarter + 1)) % half
    gathered = lax.all_gather(jnp.take(blocks, pick, axis=0), "snode", axis=0)
    other = lax.dynamic_slice_in_dim(gathered, (1 - row_position) * half, half, 0)
    partner = lax.ppermute(other[:, :quarter], "row", [(0, 1), (1, 0)])
    pool = gathered.reshape(snode_devices * (quarter + 1), width, width)
    swap = partner.reshape(half * quarter, width, width)

    u = jnp.arange(half)[:, None]
    t = jnp.arange(snode_devices)[None, :]
    near = (t // half) == row_position
    local = t % half
    d = (u - local) % half
    near_src = jnp.where(
        d <= quarter,
        (row_position * half + local) * (quarter + 1) + d,
        (row_position * half + u) * (quarter + 1) + half - d,
    )
    e = (u - local - row_position) % half
    straight = e < quarter
    far_src = ((1 - row_position) * half + local) * (quarter + 1) + jnp.where(straight, e, 0)
    src = jnp.where(near, near_src, jnp.where(straight, far_src, 0))
    far = jnp.where(near | straight, 0, u * quarter + half - 1 - e)
    pick_swap = jnp.where(near | straight, 0, 1)
    flip = jnp.where(near, d > quarter, ~straight).astype(jnp.int32)
    tables = [x.reshape(-1).astype(jnp.int32) for x in (src, far, pick_swap, flip)]

    grid_spec = pltpu.PrefetchScalarGridSpec(
        num_scalar_prefetch=4,
        grid=(snode_devices, half),
        in_specs=[
            pl.BlockSpec((1, width, width), lambda j, i, s, f, p, q: (s[i * snode_devices + j], 0, 0)),
            pl.BlockSpec((1, width, width), lambda j, i, s, f, p, q: (f[i * snode_devices + j], 0, 0)),
            pl.BlockSpec((1, width, cols), lambda j, i, s, f, p, q: (j, 0, 0)),
        ],
        out_specs=pl.BlockSpec((half * width, cols), lambda j, i, s, f, p, q: (0, 0)),
    )
    return pl.pallas_call(
        block_product_kernel,
        grid_spec=grid_spec,
        out_shape=jax.ShapeDtypeStruct((half * width, cols), jnp.float32),
    )(*tables, pool, swap, panel_rows.reshape(snode_devices, width, cols))

def body(
    ancestor_sigma,
    child_panels,
    diagonal_inverse_blocks,
    block_list,
    block_count,
    child_width,
    owner_slot,
):
    row_devices = lax.axis_size("row")
    row_positions = lax.axis_index("row")
    children = child_panels.shape[0]
    local_rows = ancestor_sigma.shape[0]
    placed, active_columns = slot_table(block_list, block_count, child_width, owner_slot)
    place_bf = placed.astype(jnp.bfloat16)
    if row_devices == 2:
        partner = lax.ppermute(child_panels, "row", [(0, 1), (1, 0)])
        ancestor_sigma, partner = lax.optimization_barrier((ancestor_sigma, partner))
        first = row_positions == 0
        gathered = jnp.concatenate(
            [jnp.where(first, child_panels, partner), jnp.where(first, partner, child_panels)], axis=1
        )
    else:
        gathered = lax.all_gather(child_panels, "row", axis=1, tiled=True)
    blocks = gathered.reshape(children, KMAX, B, WJ)
    blocks = jnp.where(active_columns[:, None, None, :], blocks, jnp.zeros_like(blocks))
    panel_rows = expand_rows(place_bf, blocks)
    snode_devices = lax.axis_size("snode")
    width = ancestor_sigma.shape[1]
    if row_devices == 2 and snode_devices % 4 == 0 and local_rows == width * snode_devices // 2:
        product = symmetric_product(
            ancestor_sigma, panel_rows, row_positions, lax.axis_index("snode"), snode_devices
        )
    else:
        flipped = lax.all_gather(ancestor_sigma.T, "snode", axis=0, tiled=True)
        product = lax.dot_general(
            flipped, panel_rows, (((0,), (0,)), ((), ())), preferred_element_type=jnp.float32
        )
    product_table = product.reshape(local_rows, children, WJ)
    own_blocks = local_rows // B
    own_table = lax.dynamic_slice_in_dim(place_bf, row_positions * own_blocks, own_blocks, 2)
    own_rows = expand_rows(own_table, blocks).reshape(local_rows, children, WJ)
    partial_value = jnp.einsum(
        "nca,ncb->cab", own_rows.astype(jnp.float32), product_table, precision=lax.Precision.HIGHEST
    )
    shared_rows = WJ // row_devices
    if row_devices == 2:
        reduced_total = partial_value + lax.ppermute(partial_value, "row", [(0, 1), (1, 0)])
    else:
        reduced_total = lax.psum(partial_value, "row")
    reduced_total = lax.dynamic_slice_in_dim(
        reduced_total, row_positions * shared_rows, shared_rows, 1
    )
    active_flags = active_columns.astype(jnp.float32)
    owned_active = lax.dynamic_slice_in_dim(
        active_flags, row_positions * shared_rows, shared_rows, 1
    )
    selected_diagonal_inverse = (
        (diagonal_inverse_blocks + reduced_total)
        * owned_active[:, :, None]
        * active_flags[:, None, :]
    )
    slot_live = jnp.sum(placed.astype(jnp.float32), axis=1)
    own_slots = lax.dynamic_slice_in_dim(slot_live, row_positions * own_blocks, own_blocks, 1)
    active_rows = jnp.repeat(own_slots.T, B, axis=0)
    selected_panel_inverse = -product_table * active_rows[:, :, None] * active_flags[None, :, :]
    return (selected_panel_inverse, selected_diagonal_inverse)


def solution(mesh):
    placed = (
        P("row", "snode"),
        P("snode", "row", None),
        P("snode", "row", None),
        P("snode", None),
        P("snode"),
        P("snode"),
        P(),
    )
    return jax.shard_map(
        body,
        mesh=mesh,
        in_specs=placed,
        out_specs=(P("row", "snode", None), P("snode", "row", None)),
        check_vma=False,
    )
```

```python
import numpy as np
import jax
import jax.numpy as jnp
from jax import lax
from jax.experimental import pallas as pl
from jax.experimental.pallas import tpu as pltpu
from jax.sharding import PartitionSpec as P

B = 128
KMAX = 32
WJ = 128
NB = 64


def slot_table(block_list, block_count, child_width, owner_slot):
    block_ids = jnp.arange(NB, dtype=jnp.int32)
    named = block_list[:, :, None] == block_ids[None, None, :]
    slot_ids = jnp.sum(jnp.where(named, owner_slot[None, None, :], 0), axis=2)
    valid_blocks = jnp.arange(KMAX, dtype=jnp.int32)[None, :] < block_count[:, None]
    placed = (slot_ids[:, :, None] == block_ids[None, None, :]) & valid_blocks[:, :, None]
    active_columns = jnp.arange(WJ, dtype=jnp.int32)[None, :] < child_width[:, None]
    return (placed, active_columns)


def expand_rows(place_table, blocks):
    children = blocks.shape[0]
    spread = jnp.einsum("ckn,ckbj->nbcj", place_table, blocks, preferred_element_type=jnp.float32)
    return spread.astype(jnp.bfloat16).reshape(place_table.shape[2] * B, children * WJ)


def block_product_kernel(src_ref, far_ref, pick_ref, flip_ref, pool_ref, swap_ref, rows_ref, out_ref):
    t = pl.program_id(0)
    u = pl.program_id(1)
    at = u * pl.num_programs(0) + t
    width = pool_ref.shape[1]
    block = jnp.where(pick_ref[at] == 0, pool_ref[0], swap_ref[0])
    block = jnp.where(flip_ref[at] == 1, block.T, block)
    contrib = jnp.dot(block, rows_ref[0], preferred_element_type=jnp.float32)
    rows = pl.ds(pl.multiple_of(u * width, width), width)

    @pl.when(t == 0)
    def _():
        out_ref[rows, :] = contrib

    @pl.when(t > 0)
    def _():
        out_ref[rows, :] += contrib


def symmetric_product(ancestor_sigma, panel_rows, row_position, snode_position, snode_devices):
    width = ancestor_sigma.shape[1]
    half = snode_devices // 2
    quarter = half // 2
    cols = panel_rows.shape[1]
    blocks = ancestor_sigma.reshape(half, width, width)
    chip_local = snode_position % half
    shift = jnp.where(snode_position // half == row_position, 0, row_position)
    pick = (chip_local + shift + jnp.arange(quarter + 1)) % half
    gathered = lax.all_gather(jnp.take(blocks, pick, axis=0), "snode", axis=0)
    other = lax.dynamic_slice_in_dim(gathered, (1 - row_position) * half, half, 0)
    partner = lax.ppermute(other[:, :quarter], "row", [(0, 1), (1, 0)])
    pool = gathered.reshape(snode_devices * (quarter + 1), width, width)
    swap = partner.reshape(half * quarter, width, width)

    u = jnp.arange(half)[:, None]
    t = jnp.arange(snode_devices)[None, :]
    near = (t // half) == row_position
    local = t % half
    d = (u - local) % half
    near_src = jnp.where(
        d <= quarter,
        (row_position * half + local) * (quarter + 1) + d,
        (row_position * half + u) * (quarter + 1) + half - d,
    )
    e = (u - local - row_position) % half
    straight = e < quarter
    far_src = ((1 - row_position) * half + local) * (quarter + 1) + jnp.where(straight, e, 0)
    src = jnp.where(near, near_src, jnp.where(straight, far_src, 0))
    far = jnp.where(near | straight, 0, u * quarter + half - 1 - e)
    pick_swap = jnp.where(near | straight, 0, 1)
    flip = jnp.where(near, d > quarter, ~straight).astype(jnp.int32)
    tables = [x.reshape(-1).astype(jnp.int32) for x in (src, far, pick_swap, flip)]

    grid_spec = pltpu.PrefetchScalarGridSpec(
        num_scalar_prefetch=4,
        grid=(snode_devices, half),
        in_specs=[
            pl.BlockSpec((1, width, width), lambda j, i, s, f, p, q: (s[i * snode_devices + j], 0, 0)),
            pl.BlockSpec((1, width, width), lambda j, i, s, f, p, q: (f[i * snode_devices + j], 0, 0)),
            pl.BlockSpec((1, width, cols), lambda j, i, s, f, p, q: (j, 0, 0)),
        ],
        out_specs=pl.BlockSpec((half * width, cols), lambda j, i, s, f, p, q: (0, 0)),
    )
    return pl.pallas_call(
        block_product_kernel,
        grid_spec=grid_spec,
        out_shape=jax.ShapeDtypeStruct((half * width, cols), jnp.float32),
    )(*tables, pool, swap, panel_rows.reshape(snode_devices, width, cols))

def body(
    ancestor_sigma,
    child_panels,
    diagonal_inverse_blocks,
    block_list,
    block_count,
    child_width,
    owner_slot,
):
    row_devices = lax.axis_size("row")
    row_positions = lax.axis_index("row")
    children = child_panels.shape[0]
    local_rows = ancestor_sigma.shape[0]
    placed, active_columns = slot_table(block_list, block_count, child_width, owner_slot)
    place_bf = placed.astype(jnp.bfloat16)
    if row_devices == 2:
        partner = lax.ppermute(child_panels, "row", [(0, 1), (1, 0)])
        ancestor_sigma, partner = lax.optimization_barrier((ancestor_sigma, partner))
        first = row_positions == 0
        gathered = jnp.concatenate(
            [jnp.where(first, child_panels, partner), jnp.where(first, partner, child_panels)], axis=1
        )
    else:
        gathered = lax.all_gather(child_panels, "row", axis=1, tiled=True)
    blocks = gathered.reshape(children, KMAX, B, WJ)
    blocks = jnp.where(active_columns[:, None, None, :], blocks, jnp.zeros_like(blocks))
    panel_rows = expand_rows(place_bf, blocks)
    snode_devices = lax.axis_size("snode")
    width = ancestor_sigma.shape[1]
    if row_devices == 2 and snode_devices % 4 == 0 and local_rows == width * snode_devices // 2:
        product = symmetric_product(
            ancestor_sigma, panel_rows, row_positions, lax.axis_index("snode"), snode_devices
        )
    else:
        flipped = lax.all_gather(ancestor_sigma.T, "snode", axis=0, tiled=True)
        product = lax.dot_general(
            flipped, panel_rows, (((0,), (0,)), ((), ())), preferred_element_type=jnp.float32
        )
    product_table = product.reshape(local_rows, children, WJ)
    own_blocks = local_rows // B
    own_table = lax.dynamic_slice_in_dim(place_bf, row_positions * own_blocks, own_blocks, 2)
    own_rows = expand_rows(own_table, blocks).reshape(local_rows, children, WJ)
    partial_value = jnp.einsum(
        "nca,ncb->cab", own_rows.astype(jnp.float32), product_table, precision=lax.Precision.HIGHEST
    )
    shared_rows = WJ // row_devices
    if row_devices == 2:
        reduced_total = partial_value + lax.ppermute(partial_value, "row", [(0, 1), (1, 0)])
    else:
        reduced_total = lax.psum(partial_value, "row")
    reduced_total = lax.dynamic_slice_in_dim(
        reduced_total, row_positions * shared_rows, shared_rows, 1
    )
    active_flags = active_columns.astype(jnp.float32)
    owned_active = lax.dynamic_slice_in_dim(
        active_flags, row_positions * shared_rows, shared_rows, 1
    )
    selected_diagonal_inverse = (
        (diagonal_inverse_blocks + reduced_total)
        * owned_active[:, :, None]
        * active_flags[:, None, :]
    )
    slot_live = jnp.sum(placed.astype(jnp.float32), axis=1)
    own_slots = lax.dynamic_slice_in_dim(slot_live, row_positions * own_blocks, own_blocks, 1)
    active_rows = jnp.repeat(own_slots.T, B, axis=0)
    selected_panel_inverse = -product_table * active_rows[:, :, None] * active_flags[None, :, :]
    return (selected_panel_inverse, selected_diagonal_inverse)


def solution(mesh):
    placed = (
        P("row", "snode"),
        P("snode", "row", None),
        P("snode", "row", None),
        P("snode", None),
        P("snode"),
        P("snode"),
        P(),
    )
    return jax.shard_map(
        body,
        mesh=mesh,
        in_specs=placed,
        out_specs=(P("row", "snode", None), P("snode", "row", None)),
        check_vma=False,
    )
```

```python
import numpy as np
import jax
import jax.numpy as jnp
from jax import lax
from jax.experimental import pallas as pl
from jax.experimental.pallas import tpu as pltpu
from jax.sharding import PartitionSpec as P

B = 128
KMAX = 32
WJ = 128
NB = 64


def slot_table(block_list, block_count, child_width, owner_slot):
    block_ids = jnp.arange(NB, dtype=jnp.int32)
    named = block_list[:, :, None] == block_ids[None, None, :]
    slot_ids = jnp.sum(jnp.where(named, owner_slot[None, None, :], 0), axis=2)
    valid_blocks = jnp.arange(KMAX, dtype=jnp.int32)[None, :] < block_count[:, None]
    placed = (slot_ids[:, :, None] == block_ids[None, None, :]) & valid_blocks[:, :, None]
    active_columns = jnp.arange(WJ, dtype=jnp.int32)[None, :] < child_width[:, None]
    return (placed, active_columns)


def expand_rows(place_table, blocks):
    children = blocks.shape[0]
    spread = jnp.einsum("ckn,ckbj->nbcj", place_table, blocks, preferred_element_type=jnp.float32)
    return spread.astype(jnp.bfloat16).reshape(place_table.shape[2] * B, children * WJ)


def block_product_kernel(src_ref, far_ref, pick_ref, flip_ref, pool_ref, swap_ref, rows_ref, out_ref):
    t = pl.program_id(0)
    u = pl.program_id(1)
    at = u * pl.num_programs(0) + t
    width = pool_ref.shape[1]
    block = jnp.where(pick_ref[at] == 0, pool_ref[0], swap_ref[0])
    block = jnp.where(flip_ref[at] == 1, block.T, block)
    contrib = jnp.dot(block, rows_ref[...], preferred_element_type=jnp.float32)
    rows = pl.ds(pl.multiple_of(u * width, width), width)

    @pl.when(t == 0)
    def _():
        out_ref[rows, :] = contrib

    @pl.when(t > 0)
    def _():
        out_ref[rows, :] += contrib


def symmetric_product(ancestor_sigma, panel_rows, row_position, snode_position, snode_devices):
    width = ancestor_sigma.shape[1]
    half = snode_devices // 2
    quarter = half // 2
    cols = panel_rows.shape[1]
    blocks = ancestor_sigma.reshape(half, width, width)
    chip_local = snode_position % half
    shift = jnp.where(snode_position // half == row_position, 0, row_position)
    pick = (chip_local + shift + jnp.arange(quarter + 1)) % half
    gathered = lax.all_gather(jnp.take(blocks, pick, axis=0), "snode", axis=0)
    other = lax.dynamic_slice_in_dim(gathered, (1 - row_position) * half, half, 0)
    partner = lax.ppermute(other[:, :quarter], "row", [(0, 1), (1, 0)])
    pool = gathered.reshape(snode_devices * (quarter + 1), width, width)
    swap = partner.reshape(half * quarter, width, width)

    u = jnp.arange(half)[:, None]
    t = jnp.arange(snode_devices)[None, :]
    near = (t // half) == row_position
    local = t % half
    d = (u - local) % half
    near_src = jnp.where(
        d <= quarter,
        (row_position * half + local) * (quarter + 1) + d,
        (row_position * half + u) * (quarter + 1) + half - d,
    )
    e = (u - local - row_position) % half
    straight = e < quarter
    far_src = ((1 - row_position) * half + local) * (quarter + 1) + jnp.where(straight, e, 0)
    src = jnp.where(near, near_src, jnp.where(straight, far_src, 0))
    far = jnp.where(near | straight, 0, u * quarter + half - 1 - e)
    pick_swap = jnp.where(near | straight, 0, 1)
    flip = jnp.where(near, d > quarter, ~straight).astype(jnp.int32)
    tables = [x.reshape(-1).astype(jnp.int32) for x in (src, far, pick_swap, flip)]

    grid_spec = pltpu.PrefetchScalarGridSpec(
        num_scalar_prefetch=4,
        grid=(snode_devices, half),
        in_specs=[
            pl.BlockSpec((1, width, width), lambda j, i, s, f, p, q: (s[i * snode_devices + j], 0, 0)),
            pl.BlockSpec((1, width, width), lambda j, i, s, f, p, q: (f[i * snode_devices + j], 0, 0)),
            pl.BlockSpec((width, cols), lambda j, i, s, f, p, q: (j, 0)),
        ],
        out_specs=pl.BlockSpec((half * width, cols), lambda j, i, s, f, p, q: (0, 0)),
    )
    return pl.pallas_call(
        block_product_kernel,
        grid_spec=grid_spec,
        out_shape=jax.ShapeDtypeStruct((half * width, cols), jnp.float32),
    )(*tables, pool, swap, panel_rows)

def body(
    ancestor_sigma,
    child_panels,
    diagonal_inverse_blocks,
    block_list,
    block_count,
    child_width,
    owner_slot,
):
    row_devices = lax.axis_size("row")
    row_positions = lax.axis_index("row")
    children = child_panels.shape[0]
    local_rows = ancestor_sigma.shape[0]
    placed, active_columns = slot_table(block_list, block_count, child_width, owner_slot)
    place_bf = placed.astype(jnp.bfloat16)
    if row_devices == 2:
        partner = lax.ppermute(child_panels, "row", [(0, 1), (1, 0)])
        ancestor_sigma, partner = lax.optimization_barrier((ancestor_sigma, partner))
        first = row_positions == 0
        gathered = jnp.concatenate(
            [jnp.where(first, child_panels, partner), jnp.where(first, partner, child_panels)], axis=1
        )
    else:
        gathered = lax.all_gather(child_panels, "row", axis=1, tiled=True)
    blocks = gathered.reshape(children, KMAX, B, WJ)
    blocks = jnp.where(active_columns[:, None, None, :], blocks, jnp.zeros_like(blocks))
    panel_rows = expand_rows(place_bf, blocks)
    snode_devices = lax.axis_size("snode")
    width = ancestor_sigma.shape[1]
    if row_devices == 2 and snode_devices % 4 == 0 and local_rows == width * snode_devices // 2:
        product = symmetric_product(
            ancestor_sigma, panel_rows, row_positions, lax.axis_index("snode"), snode_devices
        )
    else:
        flipped = lax.all_gather(ancestor_sigma.T, "snode", axis=0, tiled=True)
        product = lax.dot_general(
            flipped, panel_rows, (((0,), (0,)), ((), ())), preferred_element_type=jnp.float32
        )
    product_table = product.reshape(local_rows, children, WJ)
    own_blocks = local_rows // B
    own_table = lax.dynamic_slice_in_dim(place_bf, row_positions * own_blocks, own_blocks, 2)
    own_rows = expand_rows(own_table, blocks).reshape(local_rows, children, WJ)
    partial_value = jnp.einsum(
        "nca,ncb->cab", own_rows.astype(jnp.float32), product_table, precision=lax.Precision.HIGHEST
    )
    shared_rows = WJ // row_devices
    if row_devices == 2:
        reduced_total = partial_value + lax.ppermute(partial_value, "row", [(0, 1), (1, 0)])
    else:
        reduced_total = lax.psum(partial_value, "row")
    reduced_total = lax.dynamic_slice_in_dim(
        reduced_total, row_positions * shared_rows, shared_rows, 1
    )
    active_flags = active_columns.astype(jnp.float32)
    owned_active = lax.dynamic_slice_in_dim(
        active_flags, row_positions * shared_rows, shared_rows, 1
    )
    selected_diagonal_inverse = (
        (diagonal_inverse_blocks + reduced_total)
        * owned_active[:, :, None]
        * active_flags[:, None, :]
    )
    slot_live = jnp.sum(placed.astype(jnp.float32), axis=1)
    own_slots = lax.dynamic_slice_in_dim(slot_live, row_positions * own_blocks, own_blocks, 1)
    active_rows = jnp.repeat(own_slots.T, B, axis=0)
    selected_panel_inverse = -product_table * active_rows[:, :, None] * active_flags[None, :, :]
    return (selected_panel_inverse, selected_diagonal_inverse)


def solution(mesh):
    placed = (
        P("row", "snode"),
        P("snode", "row", None),
        P("snode", "row", None),
        P("snode", None),
        P("snode"),
        P("snode"),
        P(),
    )
    return jax.shard_map(
        body,
        mesh=mesh,
        in_specs=placed,
        out_specs=(P("row", "snode", None), P("snode", "row", None)),
        check_vma=False,
    )
```
